128 devices in a mesh: dp: 2 (over core), expert: 64 (over z, y, x).
Axes of the slice: x: 4, y: 4, z: 4, core: 2. Of those that a mesh axis runs over, the one named last changes fastest.
Arguments:
- tokens: bfloat16 [32768, 3584], P(('dp', 'expert')), may hold values from -6 to 6
- cotangent: bfloat16 [32768, 3584], P(('dp', 'expert')), may hold values from -6 to 6
- expert_ids: int32 [32768, 1], P(('dp', 'expert')), may hold values from 0 to 63; in each aligned block of 256 rows (0 to 255, 256 to 511, ...) at most 8 rows name the same one
- gate_probs: float32 [32768, 1], P(('dp', 'expert')), may hold values from 0.2 to 1
- w_gate: bfloat16 [64, 3584, 1024], P('expert', None, 'dp'), may hold values from -0.09375 to 0.09375
- w_up: bfloat16 [64, 3584, 1024], P('expert', None, 'dp'), may hold values from -0.09375 to 0.09375
- w_down: bfloat16 [64, 1024, 3584], P('expert', 'dp'), may hold values from -0.1875 to 0.1875
Outputs:
- grad_tokens: bfloat16 [32768, 3584], P(('dp', 'expert'))
- grad_gate: bfloat16 [64, 3584, 1024], P('expert', None, 'dp')
- grad_up: bfloat16 [64, 3584, 1024], P('expert', None, 'dp')
- grad_down: bfloat16 [64, 1024, 3584], P('expert', 'dp')
The draws below stay inside these ranges and needn't reach their ends.
Inputs may be any that keep to these rules, and one draw needn't show every extreme that they name: `expert_ids`: within the entries of one device's 256 tokens, no expert is named more than 8 times, and in some device one expert is named exactly 8 times. Each row names exactly one expert.
All inputs are finite; a program needn't handle non-finite values.
Results may differ from the reference program's by a relative error of at most 0.0065.
Values may be sent and summed in bfloat16 or wider, within the bound.
No kernel may reach another device: no remote copies, remote signals or barrier semaphores. Data moves between devices by JAX's collectives and lax.ppermute only.
A program may use at most 192 MiB of HBM per device.

```python
import math
import jax
import jax.numpy as jnp
import numpy as np
from jax import lax

D = 3584
F = 1024
TOPK = 1
TOK_DEV = 256
EXPERTS = 64
TOKENS = 32768
CAP = 8
N_DP = 2
N_EXPERT = 64


def shard_levels(rng, shape, split, least, high):
    def one(axis_at, blocks):
        steps = jax.random.uniform(jax.random.fold_in(jax.random.fold_in(rng, 6), axis_at), (blocks,), jnp.float32, least / len(split), high / len(split))
        return jnp.repeat(jnp.exp(steps), shape[axis_at] // blocks).reshape((-1,) + (1,) * (len(shape) - axis_at - 1))

    factor_of = one(*split[0])
    for cut in split[1:]:
        factor_of = factor_of * one(*cut)
    return factor_of


def deal_out(own_key, own, number, rows, number_of, top, most, slope):
    sequence = jax.random.permutation(own_key, number_of)
    crowded, usual = load_shares(number_of, rows * top, most, slope, True), load_shares(number_of, rows * top, most, slope, False)
    places = jnp.arange(number_of)

    def named(sizes, turn):
        used = int((sizes > 0).sum())
        fixed = max(1, used // 4)
        passed = fixed + (places - fixed + turn * (used - fixed)) % max(1, number_of - fixed)
        return jnp.zeros((number_of,), jnp.int32).at[sequence[jnp.where(places < fixed, places, passed)]].set(jnp.asarray(sizes, jnp.int32))

    sizes = jnp.where(number % 4 == 0, named(crowded, number // 4), named(usual, number - number // 4 - 1))
    mixed = jax.random.permutation(jax.random.fold_in(own, 3), number_of)
    donor, receiver = mixed[0:number_of // 2 * 2:2], mixed[1:number_of // 2 * 2:2]
    room = jnp.minimum(sizes[donor] - 1, most - sizes[receiver]) // 2
    room = jnp.where((donor == sequence[0]) | (receiver == sequence[0]) | (sizes[receiver] == 0), 0, jnp.maximum(room, 0))
    passed = jax.random.randint(jax.random.fold_in(own, 4), (number_of // 2,), 0, 1 << 20) % (room + 1)
    sizes = sizes.at[donor].add(-passed).at[receiver].add(passed)
    labels = jnp.searchsorted(jnp.cumsum(sizes), jnp.arange(rows * top), side="right").astype(jnp.int32)
    grid = labels.reshape(top, rows).T
    grid = grid[jax.random.permutation(jax.random.fold_in(own, 1), rows)]
    turn = jax.random.randint(jax.random.fold_in(own, 2), (rows, 1), 0, top)
    return jnp.take_along_axis(grid, (jnp.arange(top)[None, :] + turn) % top, axis=1)


def load_shares(count, total, bound, slope, full):
    portions = [(1 << 20) // math.isqrt(rank ** slope) + 1 for rank in range(1, count + 1)]
    largest = bound if full else min(bound, max(-(-total // count), total * portions[0] // sum(portions)))
    least = 1 if total - largest >= count - 1 else 0
    holding, spare = [largest] + [least] * (count - 1), total - largest - least * (count - 1)
    while spare > 0:
        candidates = [i for i in range(1, count) if holding[i] < largest] or [i for i in range(1, count) if holding[i] < bound]
        pool, left = sum([portions[i] for i in candidates]), spare
        for i in candidates:
            extra = min(bound - holding[i], max(1, left * portions[i] // pool), spare)
            holding[i] = holding[i] + extra
            spare = spare - extra
    return np.array(holding)


def noise(stream_key, dims, scale, reach, pieces=(), held_as=jnp.bfloat16):
    result = jax.random.normal(stream_key, dims, jnp.float32) * scale
    if len(pieces) > 0:
        result = shard_levels(stream_key, dims, pieces, -0.22, 0.18) * result
    return jnp.clip(result, min=-reach, max=reach).astype(held_as)


def setup_inputs(seed: int = 0) -> dict:
    seeds = jax.random.split(jax.random.key(seed), 8)
    tokens = noise(seeds[0], (TOKENS, D), 1.0, 6.0, ((0, 128),))
    cotangent = noise(seeds[1], (TOKENS, D), 1.0, 6.0, ((0, 128),))
    expert_ids_keys = jax.random.split(jax.random.fold_in(seeds[2], 1), TOKENS // TOK_DEV)
    expert_ids_turns = jax.random.permutation(jax.random.fold_in(seeds[2], 3), TOKENS // TOK_DEV)
    expert_ids = jax.vmap(lambda own, number: deal_out(jax.random.fold_in(seeds[2], 2), own, number, TOK_DEV, EXPERTS, TOPK, CAP, 2))(expert_ids_keys, expert_ids_turns).reshape((TOKENS, TOPK))
    gate_probs = jnp.clip(0.2 + 0.8 * jax.random.uniform(seeds[3], (TOKENS, TOPK), jnp.float32) ** shard_levels(seeds[3], (TOKENS, TOPK), ((0, 128),), -0.2, 0.2), 0.2, 1.0)
    w_gate = noise(seeds[4], (EXPERTS, D, F), D ** -0.5, 0.09375, ((0, 64), (2, 2)))
    w_up = noise(seeds[5], (EXPERTS, D, F), D ** -0.5, 0.09375, ((0, 64), (2, 2)))
    w_down = noise(seeds[6], (EXPERTS, F, D), F ** -0.5, 0.1875, ((0, 64), (1, 2)))
    return {"tokens": tokens, "cotangent": cotangent, "expert_ids": expert_ids, "gate_probs": gate_probs, "w_gate": w_gate, "w_up": w_up, "w_down": w_down}


def expert_pass(rows_x, rows_cot, gate_w, up_w, down_w):
    gate_pre = jnp.dot(rows_x, gate_w, preferred_element_type=jnp.float32)
    up_pre = jnp.dot(rows_x, up_w, preferred_element_type=jnp.float32)
    sigmoid_gate = jax.nn.sigmoid(gate_pre)
    swish_gate = gate_pre * sigmoid_gate
    hidden = (swish_gate * up_pre).astype(jnp.bfloat16)
    d_hidden = lax.dot_general(rows_cot, down_w, (((1,), (1,)), ((), ())), preferred_element_type=jnp.float32)
    d_gate = (d_hidden * up_pre * sigmoid_gate * (1.0 + gate_pre * (1.0 - sigmoid_gate))).astype(jnp.bfloat16)
    d_up = (d_hidden * swish_gate).astype(jnp.bfloat16)
    grad_down = lax.dot_general(hidden, rows_cot, (((0,), (0,)), ((), ())), preferred_element_type=jnp.float32)
    grad_gate = lax.dot_general(rows_x, d_gate, (((0,), (0,)), ((), ())), preferred_element_type=jnp.float32)
    grad_up = lax.dot_general(rows_x, d_up, (((0,), (0,)), ((), ())), preferred_element_type=jnp.float32)
    return grad_gate, grad_up, grad_down, d_gate, d_up


def reference(tokens, cotangent, expert_ids, gate_probs, w_gate, w_up, w_down):
    copies = TOKENS * TOPK
    sources = N_DP * N_EXPERT
    flat_ids = expert_ids.reshape(copies).astype(jnp.int32)
    token_of = jnp.arange(copies, dtype=jnp.int32) // TOPK
    source_of = token_of // TOK_DEV
    onehot = (flat_ids[:, None] == jnp.arange(EXPERTS, dtype=jnp.int32)[None, :]).astype(jnp.int32)
    blocked = onehot.reshape(sources, TOK_DEV * TOPK, EXPERTS)
    before = (jnp.cumsum(blocked, axis=1) - blocked).reshape(copies, EXPERTS)
    slot_rank = jnp.sum(before * onehot, axis=1).astype(jnp.int32)
    position = (source_of * CAP + slot_rank).astype(jnp.int32)
    slot_table = jnp.full((EXPERTS, sources * CAP), copies, jnp.int32)
    slot_table = slot_table.at[flat_ids, position].set(jnp.arange(copies, dtype=jnp.int32))
    copy_rows = jnp.take(tokens, token_of, axis=0)
    copy_cot = (gate_probs.reshape(copies, 1) * jnp.take(cotangent, token_of, axis=0).astype(jnp.float32)).astype(jnp.bfloat16)
    block_width = F // N_DP

    def one_expert(operands):
        index_row, gate_w, up_w, down_w = operands
        rows_x = jnp.take(copy_rows, index_row, axis=0, mode="fill", fill_value=0)
        rows_cot = jnp.take(copy_cot, index_row, axis=0, mode="fill", fill_value=0)
        grad_gate, grad_up, grad_down, d_gate, d_up = expert_pass(rows_x, rows_cot, gate_w, up_w, down_w)
        summed = jnp.zeros(rows_x.shape, jnp.float32)
        for block_index in range(N_DP):
            lower_edge = block_index * block_width
            upper_edge = lower_edge + block_width
            block_part = lax.dot_general(d_gate[:, lower_edge:upper_edge], gate_w[:, lower_edge:upper_edge], (((1,), (1,)), ((), ())), preferred_element_type=jnp.float32)
            block_part = block_part + lax.dot_general(d_up[:, lower_edge:upper_edge], up_w[:, lower_edge:upper_edge], (((1,), (1,)), ((), ())), preferred_element_type=jnp.float32)
            summed = summed + lax.optimization_barrier(block_part.astype(jnp.bfloat16)).astype(jnp.float32)
        return grad_gate.astype(jnp.bfloat16), grad_up.astype(jnp.bfloat16), grad_down.astype(jnp.bfloat16), summed.astype(jnp.bfloat16)

    grad_gate, grad_up, grad_down, copy_back = lax.map(one_expert, (slot_table, w_gate, w_up, w_down))
    copy_grad = copy_back[flat_ids, position]
    grad_tokens = jnp.sum(copy_grad.reshape(TOKENS, TOPK, D).astype(jnp.float32), axis=1).astype(jnp.bfloat16)
    return grad_tokens, grad_gate, grad_up, grad_down
```

```python
import jax
import jax.numpy as jnp
from jax import lax
from jax.sharding import PartitionSpec as P


def front_rows(rows_x, rows_cot, gate_w, up_w, down_w):
    gate_pre = jnp.dot(rows_x, gate_w, preferred_element_type=jnp.float32)
    up_pre = jnp.dot(rows_x, up_w, preferred_element_type=jnp.float32)
    sigmoid_gate = jax.nn.sigmoid(gate_pre)
    swish_gate = gate_pre * sigmoid_gate
    hidden = (swish_gate * up_pre).astype(jnp.bfloat16)
    d_hidden = lax.dot_general(
        rows_cot, down_w, (((1,), (1,)), ((), ())), preferred_element_type=jnp.float32
    )
    d_gate = (d_hidden * up_pre * sigmoid_gate * (1.0 + gate_pre * (1.0 - sigmoid_gate))).astype(
        jnp.bfloat16
    )
    d_up = (d_hidden * swish_gate).astype(jnp.bfloat16)
    dx_part = lax.dot_general(
        d_gate, gate_w, (((1,), (1,)), ((), ())), preferred_element_type=jnp.float32
    )
    dx_part = dx_part + lax.dot_general(
        d_up, up_w, (((1,), (1,)), ((), ())), preferred_element_type=jnp.float32
    )
    return (hidden, d_gate, d_up, dx_part.astype(jnp.bfloat16))


def weight_sums(rows_x, rows_cot, hidden, d_gate, d_up):
    grad_gate = lax.dot_general(
        rows_x, d_gate, (((0,), (0,)), ((), ())), preferred_element_type=jnp.float32
    )
    grad_up = lax.dot_general(
        rows_x, d_up, (((0,), (0,)), ((), ())), preferred_element_type=jnp.float32
    )
    grad_down = lax.dot_general(
        hidden, rows_cot, (((0,), (0,)), ((), ())), preferred_element_type=jnp.float32
    )
    return (grad_gate, grad_up, grad_down)


def live_of(counts_three, capacity):
    return (jnp.arange(capacity, dtype=jnp.int32) < counts_three).reshape(-1)


def tile_flags(counts_three, capacity):
    live_rows = live_of(counts_three, capacity).astype(jnp.int32)
    return jnp.max(live_rows.reshape(-1, 128), axis=1) > 0


def run_front(rows_four, cots_four, counts_three, weights, capacity):
    model_width = rows_four.shape[-1]
    rows_flat = rows_four.reshape(-1, model_width)
    cots_flat = cots_four.reshape(-1, model_width)
    slot_count = rows_flat.shape[0]
    hidden_width = weights[0].shape[1]
    spare_rows = -slot_count % 128
    tiles_all = (slot_count + spare_rows) // 128
    flags = tile_flags(counts_three, capacity)

    def empty_tile():
        return (
            jnp.zeros((128, hidden_width), jnp.bfloat16),
            jnp.zeros((128, hidden_width), jnp.bfloat16),
            jnp.zeros((128, hidden_width), jnp.bfloat16),
            jnp.zeros((128, model_width), jnp.bfloat16),
        )

    def add_tile(index_tile, outputs):
        start = index_tile * 128
        tile_x = lax.dynamic_slice_in_dim(rows_flat, start, 128)
        tile_cot = lax.dynamic_slice_in_dim(cots_flat, start, 128)
        tile_out = lax.cond(
            flags[index_tile],
            lambda: front_rows(tile_x, tile_cot, weights[0], weights[1], weights[2]),
            empty_tile,
        )
        return tuple(
            (
                lax.dynamic_update_slice_in_dim(whole, piece, start, 0)
                for whole, piece in zip(outputs, tile_out)
            )
        )

    total_rows = slot_count + spare_rows
    initial = (
        jnp.zeros((total_rows, hidden_width), jnp.bfloat16),
        jnp.zeros((total_rows, hidden_width), jnp.bfloat16),
        jnp.zeros((total_rows, hidden_width), jnp.bfloat16),
        jnp.zeros((total_rows, model_width), jnp.bfloat16),
    )
    outputs = lax.fori_loop(0, tiles_all, add_tile, initial)
    results = tuple((whole for whole in outputs))
    return results


def run_sums(rows_x, rows_cot, hidden, d_gate, d_up, counts_three, capacity):
    slot_count = rows_x.shape[0]
    model_width = rows_x.shape[1]
    hidden_width = hidden.shape[1]
    spare_rows = -slot_count % 128
    tiles_all = (slot_count + spare_rows) // 128
    sources = [source for source in (rows_x, rows_cot, hidden, d_gate, d_up)]
    flags = tile_flags(counts_three, capacity)

    def add_tile(index_tile, totals):
        start = index_tile * 128
        operands = [lax.dynamic_slice_in_dim(source, start, 128) for source in sources]

        def with_tile():
            added = weight_sums(operands[0], operands[1], operands[2], operands[3], operands[4])
            return tuple((running + extra for running, extra in zip(totals, added)))

        return lax.cond(flags[index_tile], with_tile, lambda: totals)

    initial = (
        jnp.zeros((model_width, hidden_width), jnp.float32),
        jnp.zeros((model_width, hidden_width), jnp.float32),
        jnp.zeros((hidden_width, model_width), jnp.float32),
    )
    sums = lax.fori_loop(0, tiles_all, add_tile, initial)
    return sums


def local(tokens, cotangent, expert_ids, gate_probs, w_gate, w_up, w_down):
    owners = lax.axis_size("expert")
    groups = lax.axis_size("dp")
    tok_rows = tokens.shape[0]
    model_width = tokens.shape[1]
    fanout = expert_ids.shape[1]
    capacity = max(2, 2 * tok_rows * fanout // owners)
    copies = tok_rows * fanout
    flat_ids = expert_ids.reshape(copies)
    onehot = (flat_ids[:, None] == jnp.arange(owners, dtype=jnp.int32)[None, :]).astype(jnp.int32)
    before = jnp.cumsum(onehot, axis=0) - onehot
    slot_rank = jnp.sum(before * onehot, axis=1)
    counts = jnp.sum(onehot, axis=0).reshape(owners, 1)
    position = flat_ids * capacity + slot_rank
    copy_rows = tokens[:, None, :].reshape(copies, model_width)
    copy_tok_cot = cotangent[:, None, :].reshape(copies, model_width)
    copy_cots = (gate_probs * copy_tok_cot.astype(jnp.float32)).astype(jnp.bfloat16)
    placing = (jnp.arange(owners * capacity, dtype=jnp.int32)[:, None] == position[None, :]).astype(
        jnp.bfloat16
    )
    sent_rows = (
        jnp.dot(placing, copy_rows, preferred_element_type=jnp.float32)
        .astype(jnp.bfloat16)
        .reshape(owners, capacity, model_width)
    )
    sent_cots = (
        jnp.dot(placing, copy_cots, preferred_element_type=jnp.float32)
        .astype(jnp.bfloat16)
        .reshape(owners, capacity, model_width)
    )
    came_rows, came_cots, came_counts = (
        lax.all_to_all(sent_rows, "expert", split_axis=0, concat_axis=0, tiled=True),
        lax.all_to_all(sent_cots, "expert", split_axis=0, concat_axis=0, tiled=True),
        lax.all_to_all(counts, "expert", split_axis=0, concat_axis=0, tiled=True),
    )
    got_rows, got_cots, got_counts = (
        lax.all_gather(came_rows, "dp", axis=0, tiled=True),
        lax.all_gather(came_cots, "dp", axis=0, tiled=True),
        lax.all_gather(came_counts, "dp", axis=0, tiled=True),
    )
    got_rows = got_rows.reshape(groups, owners, capacity, model_width)
    got_cots = got_cots.reshape(groups, owners, capacity, model_width)
    got_counts = got_counts.reshape(groups, owners, 1)
    slots_all = owners * groups * capacity
    weights_own = (w_gate[0], w_up[0], w_down[0])
    rows_x = got_rows.reshape(slots_all, model_width)
    rows_cot = got_cots.reshape(slots_all, model_width)
    hidden, d_gate, d_up, dx_part = front_rows(rows_x, rows_cot, *weights_own)
    grad_gate, grad_up, grad_down = weight_sums(rows_x, rows_cot, hidden, d_gate, d_up)
    dx_float = dx_part.astype(jnp.float32)
    summed = lax.psum_scatter(
        dx_float.reshape(groups * owners, capacity, model_width).astype(jnp.bfloat16),
        "dp",
        scatter_dimension=0,
        tiled=True,
    )
    returned = lax.all_to_all(summed, "expert", split_axis=0, concat_axis=0, tiled=True)
    copy_grad = lax.dot_general(
        placing,
        returned.reshape(owners * capacity, model_width),
        (((0,), (0,)), ((), ())),
        preferred_element_type=jnp.float32,
    )
    grad_tokens = jnp.sum(copy_grad.reshape(tok_rows, fanout, model_width), axis=1).astype(
        jnp.bfloat16
    )
    return (
        grad_tokens,
        grad_gate.astype(jnp.bfloat16)[None],
        grad_up.astype(jnp.bfloat16)[None],
        grad_down.astype(jnp.bfloat16)[None],
    )


def solution(mesh):
    return jax.shard_map(
        local,
        mesh=mesh,
        in_specs=(
            P(("dp", "expert"), None),
            P(("dp", "expert"), None),
            P(("dp", "expert"), None),
            P(("dp", "expert"), None),
            P("expert", None, "dp"),
            P("expert", None, "dp"),
            P("expert", "dp", None),
        ),
        out_specs=(
            P(("dp", "expert"), None),
            P("expert", None, "dp"),
            P("expert", None, "dp"),
            P("expert", "dp", None),
        ),
        check_vma=False,
    )
```

```python
import jax
import jax.numpy as jnp
from jax import lax
from jax.sharding import PartitionSpec as P


def front_rows(rows_x, rows_cot, gate_w, up_w, down_w):
    gate_pre = jnp.dot(rows_x, gate_w, preferred_element_type=jnp.float32)
    up_pre = jnp.dot(rows_x, up_w, preferred_element_type=jnp.float32)
    sigmoid_gate = jax.nn.sigmoid(gate_pre)
    swish_gate = gate_pre * sigmoid_gate
    hidden = (swish_gate * up_pre).astype(jnp.bfloat16)
    d_hidden = lax.dot_general(
        rows_cot, down_w, (((1,), (1,)), ((), ())), preferred_element_type=jnp.float32
    )
    d_gate = (d_hidden * up_pre * sigmoid_gate * (1.0 + gate_pre * (1.0 - sigmoid_gate))).astype(
        jnp.bfloat16
    )
    d_up = (d_hidden * swish_gate).astype(jnp.bfloat16)
    dx_part = lax.dot_general(
        d_gate, gate_w, (((1,), (1,)), ((), ())), preferred_element_type=jnp.float32
    )
    dx_part = dx_part + lax.dot_general(
        d_up, up_w, (((1,), (1,)), ((), ())), preferred_element_type=jnp.float32
    )
    return (hidden, d_gate, d_up, dx_part.astype(jnp.bfloat16))


def weight_sums(rows_x, rows_cot, hidden, d_gate, d_up):
    grad_gate = lax.dot_general(
        rows_x, d_gate, (((0,), (0,)), ((), ())), preferred_element_type=jnp.float32
    )
    grad_up = lax.dot_general(
        rows_x, d_up, (((0,), (0,)), ((), ())), preferred_element_type=jnp.float32
    )
    grad_down = lax.dot_general(
        hidden, rows_cot, (((0,), (0,)), ((), ())), preferred_element_type=jnp.float32
    )
    return (grad_gate, grad_up, grad_down)


def live_of(counts_three, capacity):
    return (jnp.arange(capacity, dtype=jnp.int32) < counts_three).reshape(-1)


def tile_flags(counts_three, capacity):
    live_rows = live_of(counts_three, capacity).astype(jnp.int32)
    return jnp.max(live_rows.reshape(-1, 128), axis=1) > 0


def run_front(rows_four, cots_four, counts_three, weights, capacity):
    model_width = rows_four.shape[-1]
    rows_flat = rows_four.reshape(-1, model_width)
    cots_flat = cots_four.reshape(-1, model_width)
    slot_count = rows_flat.shape[0]
    hidden_width = weights[0].shape[1]
    spare_rows = -slot_count % 128
    tiles_all = (slot_count + spare_rows) // 128
    flags = tile_flags(counts_three, capacity)

    def empty_tile():
        return (
            jnp.zeros((128, hidden_width), jnp.bfloat16),
            jnp.zeros((128, hidden_width), jnp.bfloat16),
            jnp.zeros((128, hidden_width), jnp.bfloat16),
            jnp.zeros((128, model_width), jnp.bfloat16),
        )

    def add_tile(index_tile, outputs):
        start = index_tile * 128
        tile_x = lax.dynamic_slice_in_dim(rows_flat, start, 128)
        tile_cot = lax.dynamic_slice_in_dim(cots_flat, start, 128)
        tile_out = lax.cond(
            flags[index_tile],
            lambda: front_rows(tile_x, tile_cot, weights[0], weights[1], weights[2]),
            empty_tile,
        )
        return tuple(
            (
                lax.dynamic_update_slice_in_dim(whole, piece, start, 0)
                for whole, piece in zip(outputs, tile_out)
            )
        )

    total_rows = slot_count + spare_rows
    initial = (
        jnp.zeros((total_rows, hidden_width), jnp.bfloat16),
        jnp.zeros((total_rows, hidden_width), jnp.bfloat16),
        jnp.zeros((total_rows, hidden_width), jnp.bfloat16),
        jnp.zeros((total_rows, model_width), jnp.bfloat16),
    )
    outputs = lax.fori_loop(0, tiles_all, add_tile, initial)
    results = tuple((whole for whole in outputs))
    return results


def run_sums(rows_x, rows_cot, hidden, d_gate, d_up, counts_three, capacity):
    slot_count = rows_x.shape[0]
    model_width = rows_x.shape[1]
    hidden_width = hidden.shape[1]
    spare_rows = -slot_count % 128
    tiles_all = (slot_count + spare_rows) // 128
    sources = [source for source in (rows_x, rows_cot, hidden, d_gate, d_up)]
    flags = tile_flags(counts_three, capacity)

    def add_tile(index_tile, totals):
        start = index_tile * 128
        operands = [lax.dynamic_slice_in_dim(source, start, 128) for source in sources]

        def with_tile():
            added = weight_sums(operands[0], operands[1], operands[2], operands[3], operands[4])
            return tuple((running + extra for running, extra in zip(totals, added)))

        return lax.cond(flags[index_tile], with_tile, lambda: totals)

    initial = (
        jnp.zeros((model_width, hidden_width), jnp.float32),
        jnp.zeros((model_width, hidden_width), jnp.float32),
        jnp.zeros((hidden_width, model_width), jnp.float32),
    )
    sums = lax.fori_loop(0, tiles_all, add_tile, initial)
    return sums


def local(tokens, cotangent, expert_ids, gate_probs, w_gate, w_up, w_down):
    owners = lax.axis_size("expert")
    groups = lax.axis_size("dp")
    tok_rows = tokens.shape[0]
    model_width = tokens.shape[1]
    fanout = expert_ids.shape[1]
    capacity = max(2, 2 * tok_rows * fanout // owners)
    copies = tok_rows * fanout
    flat_ids = expert_ids.reshape(copies)
    onehot = (flat_ids[:, None] == jnp.arange(owners, dtype=jnp.int32)[None, :]).astype(jnp.int32)
    before = jnp.cumsum(onehot, axis=0) - onehot
    slot_rank = jnp.sum(before * onehot, axis=1)
    position = flat_ids * capacity + slot_rank
    copy_rows = tokens[:, None, :].reshape(copies, model_width)
    copy_tok_cot = cotangent[:, None, :].reshape(copies, model_width)
    copy_cots = (gate_probs * copy_tok_cot.astype(jnp.float32)).astype(jnp.bfloat16)
    placing = (jnp.arange(owners * capacity, dtype=jnp.int32)[:, None] == position[None, :]).astype(
        jnp.bfloat16
    )
    stacked = jnp.stack([copy_rows, copy_cots], axis=1)
    sent = (
        jnp.einsum("pc,cxd->pxd", placing, stacked, preferred_element_type=jnp.float32)
        .astype(jnp.bfloat16)
        .reshape(owners, capacity, 2, model_width)
    )
    came = lax.all_to_all(sent, "expert", split_axis=0, concat_axis=0, tiled=True)
    swap = [(0, 1), (1, 0)]
    other = lax.ppermute(came, "dp", swap)
    half_slots = owners * capacity
    weights_own = (w_gate[0], w_up[0], w_down[0])
    own_x = came[:, :, 0].reshape(half_slots, model_width)
    own_cot = came[:, :, 1].reshape(half_slots, model_width)
    own_h, own_dg, own_du, own_dx = front_rows(own_x, own_cot, *weights_own)
    oth_x = other[:, :, 0].reshape(half_slots, model_width)
    oth_cot = other[:, :, 1].reshape(half_slots, model_width)
    oth_h, oth_dg, oth_du, oth_dx = front_rows(oth_x, oth_cot, *weights_own)
    back = lax.ppermute(oth_dx, "dp", swap)
    summed = (own_dx.astype(jnp.float32) + back.astype(jnp.float32)).astype(jnp.bfloat16)
    returned = lax.all_to_all(
        summed.reshape(owners, capacity, model_width), "expert", split_axis=0, concat_axis=0, tiled=True
    )
    sums_own = weight_sums(own_x, own_cot, own_h, own_dg, own_du)
    sums_oth = weight_sums(oth_x, oth_cot, oth_h, oth_dg, oth_du)
    grad_gate, grad_up, grad_down = (a + b for a, b in zip(sums_own, sums_oth))
    copy_grad = lax.dot_general(
        placing,
        returned.reshape(owners * capacity, model_width),
        (((0,), (0,)), ((), ())),
        preferred_element_type=jnp.float32,
    )
    grad_tokens = jnp.sum(copy_grad.reshape(tok_rows, fanout, model_width), axis=1).astype(
        jnp.bfloat16
    )
    return (
        grad_tokens,
        grad_gate.astype(jnp.bfloat16)[None],
        grad_up.astype(jnp.bfloat16)[None],
        grad_down.astype(jnp.bfloat16)[None],
    )


def solution(mesh):
    return jax.shard_map(
        local,
        mesh=mesh,
        in_specs=(
            P(("dp", "expert"), None),
            P(("dp", "expert"), None),
            P(("dp", "expert"), None),
            P(("dp", "expert"), None),
            P("expert", None, "dp"),
            P("expert", None, "dp"),
            P("expert", "dp", None),
        ),
        out_specs=(
            P(("dp", "expert"), None),
            P("expert", None, "dp"),
            P("expert", None, "dp"),
            P("expert", "dp", None),
        ),
        check_vma=False,
    )
```

```python
import jax
import jax.numpy as jnp
from jax import lax
from jax.sharding import PartitionSpec as P


def front_rows(rows_x, rows_cot, gate_w, up_w, down_w):
    gate_pre = jnp.dot(rows_x, gate_w, preferred_element_type=jnp.float32)
    up_pre = jnp.dot(rows_x, up_w, preferred_element_type=jnp.float32)
    sigmoid_gate = jax.nn.sigmoid(gate_pre)
    swish_gate = gate_pre * sigmoid_gate
    hidden = (swish_gate * up_pre).astype(jnp.bfloat16)
    d_hidden = lax.dot_general(
        rows_cot, down_w, (((1,), (1,)), ((), ())), preferred_element_type=jnp.float32
    )
    d_gate = (d_hidden * up_pre * sigmoid_gate * (1.0 + gate_pre * (1.0 - sigmoid_gate))).astype(
        jnp.bfloat16
    )
    d_up = (d_hidden * swish_gate).astype(jnp.bfloat16)
    dx_part = lax.dot_general(
        d_gate, gate_w, (((1,), (1,)), ((), ())), preferred_element_type=jnp.float32
    )
    dx_part = dx_part + lax.dot_general(
        d_up, up_w, (((1,), (1,)), ((), ())), preferred_element_type=jnp.float32
    )
    return (hidden, d_gate, d_up, dx_part.astype(jnp.bfloat16))


def weight_sums(rows_x, rows_cot, hidden, d_gate, d_up):
    grad_gate = lax.dot_general(
        rows_x, d_gate, (((0,), (0,)), ((), ())), preferred_element_type=jnp.float32
    )
    grad_up = lax.dot_general(
        rows_x, d_up, (((0,), (0,)), ((), ())), preferred_element_type=jnp.float32
    )
    grad_down = lax.dot_general(
        hidden, rows_cot, (((0,), (0,)), ((), ())), preferred_element_type=jnp.float32
    )
    return (grad_gate, grad_up, grad_down)


def live_of(counts_three, capacity):
    return (jnp.arange(capacity, dtype=jnp.int32) < counts_three).reshape(-1)


def tile_flags(counts_three, capacity):
    live_rows = live_of(counts_three, capacity).astype(jnp.int32)
    return jnp.max(live_rows.reshape(-1, 128), axis=1) > 0


def run_front(rows_four, cots_four, counts_three, weights, capacity):
    model_width = rows_four.shape[-1]
    rows_flat = rows_four.reshape(-1, model_width)
    cots_flat = cots_four.reshape(-1, model_width)
    slot_count = rows_flat.shape[0]
    hidden_width = weights[0].shape[1]
    spare_rows = -slot_count % 128
    tiles_all = (slot_count + spare_rows) // 128
    flags = tile_flags(counts_three, capacity)

    def empty_tile():
        return (
            jnp.zeros((128, hidden_width), jnp.bfloat16),
            jnp.zeros((128, hidden_width), jnp.bfloat16),
            jnp.zeros((128, hidden_width), jnp.bfloat16),
            jnp.zeros((128, model_width), jnp.bfloat16),
        )

    def add_tile(index_tile, outputs):
        start = index_tile * 128
        tile_x = lax.dynamic_slice_in_dim(rows_flat, start, 128)
        tile_cot = lax.dynamic_slice_in_dim(cots_flat, start, 128)
        tile_out = lax.cond(
            flags[index_tile],
            lambda: front_rows(tile_x, tile_cot, weights[0], weights[1], weights[2]),
            empty_tile,
        )
        return tuple(
            (
                lax.dynamic_update_slice_in_dim(whole, piece, start, 0)
                for whole, piece in zip(outputs, tile_out)
            )
        )

    total_rows = slot_count + spare_rows
    initial = (
        jnp.zeros((total_rows, hidden_width), jnp.bfloat16),
        jnp.zeros((total_rows, hidden_width), jnp.bfloat16),
        jnp.zeros((total_rows, hidden_width), jnp.bfloat16),
        jnp.zeros((total_rows, model_width), jnp.bfloat16),
    )
    outputs = lax.fori_loop(0, tiles_all, add_tile, initial)
    results = tuple((whole for whole in outputs))
    return results


def run_sums(rows_x, rows_cot, hidden, d_gate, d_up, counts_three, capacity):
    slot_count = rows_x.shape[0]
    model_width = rows_x.shape[1]
    hidden_width = hidden.shape[1]
    spare_rows = -slot_count % 128
    tiles_all = (slot_count + spare_rows) // 128
    sources = [source for source in (rows_x, rows_cot, hidden, d_gate, d_up)]
    flags = tile_flags(counts_three, capacity)

    def add_tile(index_tile, totals):
        start = index_tile * 128
        operands = [lax.dynamic_slice_in_dim(source, start, 128) for source in sources]

        def with_tile():
            added = weight_sums(operands[0], operands[1], operands[2], operands[3], operands[4])
            return tuple((running + extra for running, extra in zip(totals, added)))

        return lax.cond(flags[index_tile], with_tile, lambda: totals)

    initial = (
        jnp.zeros((model_width, hidden_width), jnp.float32),
        jnp.zeros((model_width, hidden_width), jnp.float32),
        jnp.zeros((hidden_width, model_width), jnp.float32),
    )
    sums = lax.fori_loop(0, tiles_all, add_tile, initial)
    return sums


def local(tokens, cotangent, expert_ids, gate_probs, w_gate, w_up, w_down):
    owners = lax.axis_size("expert")
    tok_rows = tokens.shape[0]
    model_width = tokens.shape[1]
    fanout = expert_ids.shape[1]
    capacity = max(2, 2 * tok_rows * fanout // owners)
    chunks = 2
    per_chunk = capacity // chunks
    copies = tok_rows * fanout
    flat_ids = expert_ids.reshape(copies)
    onehot = (flat_ids[:, None] == jnp.arange(owners, dtype=jnp.int32)[None, :]).astype(jnp.int32)
    before = jnp.cumsum(onehot, axis=0) - onehot
    slot_rank = jnp.sum(before * onehot, axis=1)
    copy_rows = tokens[:, None, :].reshape(copies, model_width)
    copy_tok_cot = cotangent[:, None, :].reshape(copies, model_width)
    copy_cots = (gate_probs * copy_tok_cot.astype(jnp.float32)).astype(jnp.bfloat16)
    stacked = jnp.stack([copy_rows, copy_cots], axis=1)
    swap = [(0, 1), (1, 0)]
    weights_own = (w_gate[0], w_up[0], w_down[0])
    chunk_slots = owners * per_chunk
    pieces = []
    placings = []
    returns = []
    for chunk in range(chunks):
        position = flat_ids * per_chunk + (slot_rank - chunk * per_chunk)
        in_chunk = (slot_rank >= chunk * per_chunk) & (slot_rank < (chunk + 1) * per_chunk)
        position = jnp.where(in_chunk, position, -1)
        placing = (
            jnp.arange(chunk_slots, dtype=jnp.int32)[:, None] == position[None, :]
        ).astype(jnp.bfloat16)
        placings.append(placing)
        sent = (
            jnp.einsum("pc,cxd->pxd", placing, stacked, preferred_element_type=jnp.float32)
            .astype(jnp.bfloat16)
            .reshape(owners, per_chunk, 2, model_width)
        )
        came = lax.all_to_all(sent, "expert", split_axis=0, concat_axis=0, tiled=True)
        other = lax.ppermute(came, "dp", swap)
        own_x = came[:, :, 0].reshape(chunk_slots, model_width)
        own_cot = came[:, :, 1].reshape(chunk_slots, model_width)
        own_h, own_dg, own_du, own_dx = front_rows(own_x, own_cot, *weights_own)
        oth_x = other[:, :, 0].reshape(chunk_slots, model_width)
        oth_cot = other[:, :, 1].reshape(chunk_slots, model_width)
        oth_h, oth_dg, oth_du, oth_dx = front_rows(oth_x, oth_cot, *weights_own)
        back = lax.ppermute(oth_dx, "dp", swap)
        own_dx = lax.optimization_barrier(own_dx)
        summed = (own_dx.astype(jnp.float32) + back.astype(jnp.float32)).astype(jnp.bfloat16)
        returned = lax.all_to_all(
            summed.reshape(owners, per_chunk, model_width),
            "expert",
            split_axis=0,
            concat_axis=0,
            tiled=True,
        )
        returns.append(returned.reshape(chunk_slots, model_width))
        pieces.append((own_x, own_cot, own_h, own_dg, own_du))
        pieces.append((oth_x, oth_cot, oth_h, oth_dg, oth_du))
    joined = [jnp.concatenate(part, axis=0) for part in zip(*pieces)]
    grad_gate, grad_up, grad_down = weight_sums(*joined)
    copy_grad = sum(
        lax.dot_general(
            placing, returned, (((0,), (0,)), ((), ())), preferred_element_type=jnp.float32
        )
        for placing, returned in zip(placings, returns)
    )
    grad_tokens = jnp.sum(copy_grad.reshape(tok_rows, fanout, model_width), axis=1).astype(
        jnp.bfloat16
    )
    return (
        grad_tokens,
        grad_gate.astype(jnp.bfloat16)[None],
        grad_up.astype(jnp.bfloat16)[None],
        grad_down.astype(jnp.bfloat16)[None],
    )


def solution(mesh):
    return jax.shard_map(
        local,
        mesh=mesh,
        in_specs=(
            P(("dp", "expert"), None),
            P(("dp", "expert"), None),
            P(("dp", "expert"), None),
            P(("dp", "expert"), None),
            P("expert", None, "dp"),
            P("expert", None, "dp"),
            P("expert", "dp", None),
        ),
        out_specs=(
            P(("dp", "expert"), None),
            P("expert", None, "dp"),
            P("expert", None, "dp"),
            P("expert", "dp", None),
        ),
        check_vma=False,
    )
```

```python
import jax
import jax.numpy as jnp
from jax import lax
from jax.sharding import PartitionSpec as P


def front_rows(rows_x, rows_cot, gate_w, up_w, down_w):
    gate_pre = jnp.dot(rows_x, gate_w, preferred_element_type=jnp.float32)
    up_pre = jnp.dot(rows_x, up_w, preferred_element_type=jnp.float32)
    sigmoid_gate = jax.nn.sigmoid(gate_pre)
    swish_gate = gate_pre * sigmoid_gate
    hidden = (swish_gate * up_pre).astype(jnp.bfloat16)
    d_hidden = lax.dot_general(
        rows_cot, down_w, (((1,), (1,)), ((), ())), preferred_element_type=jnp.float32
    )
    d_gate = (d_hidden * up_pre * sigmoid_gate * (1.0 + gate_pre * (1.0 - sigmoid_gate))).astype(
        jnp.bfloat16
    )
    d_up = (d_hidden * swish_gate).astype(jnp.bfloat16)
    return (hidden, d_gate, d_up, input_grads(d_gate, d_up, gate_w, up_w))


def input_grads(d_gate, d_up, gate_w, up_w):
    dx_part = lax.dot_general(
        d_gate, gate_w, (((1,), (1,)), ((), ())), preferred_element_type=jnp.float32
    )
    dx_part = dx_part + lax.dot_general(
        d_up, up_w, (((1,), (1,)), ((), ())), preferred_element_type=jnp.float32
    )
    return dx_part.astype(jnp.bfloat16)


def weight_sums(rows_x, rows_cot, hidden, d_gate, d_up):
    grad_gate = lax.dot_general(
        rows_x, d_gate, (((0,), (0,)), ((), ())), preferred_element_type=jnp.float32
    )
    grad_up = lax.dot_general(
        rows_x, d_up, (((0,), (0,)), ((), ())), preferred_element_type=jnp.float32
    )
    grad_down = lax.dot_general(
        hidden, rows_cot, (((0,), (0,)), ((), ())), preferred_element_type=jnp.float32
    )
    return (grad_gate, grad_up, grad_down)


def local(tokens, cotangent, expert_ids, gate_probs, w_gate, w_up, w_down):
    owners = lax.axis_size("expert")
    tok_rows = tokens.shape[0]
    model_width = tokens.shape[1]
    fanout = expert_ids.shape[1]
    capacity = max(2, 2 * tok_rows * fanout // owners)
    copies = tok_rows * fanout
    flat_ids = expert_ids.reshape(copies)
    onehot = (flat_ids[:, None] == jnp.arange(owners, dtype=jnp.int32)[None, :]).astype(jnp.int32)
    before = jnp.cumsum(onehot, axis=0) - onehot
    slot_rank = jnp.sum(before * onehot, axis=1)
    position = flat_ids * capacity + slot_rank
    copy_rows = tokens[:, None, :].reshape(copies, model_width)
    copy_tok_cot = cotangent[:, None, :].reshape(copies, model_width)
    copy_cots = (gate_probs * copy_tok_cot.astype(jnp.float32)).astype(jnp.bfloat16)
    placing = (jnp.arange(owners * capacity, dtype=jnp.int32)[:, None] == position[None, :]).astype(
        jnp.bfloat16
    )
    joined = jnp.concatenate([copy_rows, copy_cots], axis=1)
    sent = (
        jnp.dot(placing, joined, preferred_element_type=jnp.float32)
        .astype(jnp.bfloat16)
        .reshape(owners, capacity, 2 * model_width)
    )
    came = lax.all_to_all(sent, "expert", split_axis=0, concat_axis=0, tiled=True)
    swap = [(0, 1), (1, 0)]
    other = lax.ppermute(came, "dp", swap)
    half_slots = owners * capacity
    weights_own = (w_gate[0], w_up[0], w_down[0])
    came = came.reshape(half_slots, 2 * model_width)
    own_x = came[:, :model_width]
    own_cot = came[:, model_width:]
    own_h, own_dg, own_du = front_rows(own_x, own_cot, *weights_own)[:3]
    other = other.reshape(half_slots, 2 * model_width)
    oth_x = other[:, :model_width]
    oth_cot = other[:, model_width:]
    oth_h, oth_dg, oth_du, oth_dx = front_rows(oth_x, oth_cot, *weights_own)
    back = lax.ppermute(oth_dx, "dp", swap)
    own_dx = lax.optimization_barrier(input_grads(own_dg, own_du, weights_own[0], weights_own[1]))
    summed = (own_dx.astype(jnp.float32) + back.astype(jnp.float32)).astype(jnp.bfloat16)
    returned = lax.all_to_all(
        summed.reshape(owners, capacity, model_width), "expert", split_axis=0, concat_axis=0, tiled=True
    )
    sums_own = weight_sums(own_x, own_cot, own_h, own_dg, own_du)
    sums_oth = weight_sums(oth_x, oth_cot, oth_h, oth_dg, oth_du)
    grad_gate, grad_up, grad_down = (a + b for a, b in zip(sums_own, sums_oth))
    copy_grad = lax.dot_general(
        placing,
        returned.reshape(owners * capacity, model_width),
        (((0,), (0,)), ((), ())),
        preferred_element_type=jnp.float32,
    )
    grad_tokens = jnp.sum(copy_grad.reshape(tok_rows, fanout, model_width), axis=1).astype(
        jnp.bfloat16
    )
    return (
        grad_tokens,
        grad_gate.astype(jnp.bfloat16)[None],
        grad_up.astype(jnp.bfloat16)[None],
        grad_down.astype(jnp.bfloat16)[None],
    )


def solution(mesh):
    return jax.shard_map(
        local,
        mesh=mesh,
        in_specs=(
            P(("dp", "expert"), None),
            P(("dp", "expert"), None),
            P(("dp", "expert"), None),
            P(("dp", "expert"), None),
            P("expert", None, "dp"),
            P("expert", None, "dp"),
            P("expert", "dp", None),
        ),
        out_specs=(
            P(("dp", "expert"), None),
            P("expert", None, "dp"),
            P("expert", None, "dp"),
            P("expert", "dp", None),
        ),
        check_vma=False,
    )
```

```python
import jax
import jax.numpy as jnp
from jax import lax
from jax.sharding import PartitionSpec as P


def front_rows(rows_x, rows_cot, gate_w, up_w, down_w):
    gate_pre = jnp.dot(rows_x, gate_w, preferred_element_type=jnp.float32)
    up_pre = jnp.dot(rows_x, up_w, preferred_element_type=jnp.float32)
    sigmoid_gate = jax.nn.sigmoid(gate_pre)
    swish_gate = gate_pre * sigmoid_gate
    hidden = (swish_gate * up_pre).astype(jnp.bfloat16)
    d_hidden = lax.dot_general(
        rows_cot, down_w, (((1,), (1,)), ((), ())), preferred_element_type=jnp.float32
    )
    d_gate = (d_hidden * up_pre * sigmoid_gate * (1.0 + gate_pre * (1.0 - sigmoid_gate))).astype(
        jnp.bfloat16
    )
    d_up = (d_hidden * swish_gate).astype(jnp.bfloat16)
    return (hidden, d_gate, d_up, input_grads(d_gate, d_up, gate_w, up_w))


def input_grads(d_gate, d_up, gate_w, up_w):
    dx_part = lax.dot_general(
        d_gate, gate_w, (((1,), (1,)), ((), ())), preferred_element_type=jnp.float32
    )
    dx_part = dx_part + lax.dot_general(
        d_up, up_w, (((1,), (1,)), ((), ())), preferred_element_type=jnp.float32
    )
    return dx_part.astype(jnp.bfloat16)


def weight_sums(rows_x, rows_cot, hidden, d_gate, d_up):
    grad_gate = lax.dot_general(
        rows_x, d_gate, (((0,), (0,)), ((), ())), preferred_element_type=jnp.float32
    )
    grad_up = lax.dot_general(
        rows_x, d_up, (((0,), (0,)), ((), ())), preferred_element_type=jnp.float32
    )
    grad_down = lax.dot_general(
        hidden, rows_cot, (((0,), (0,)), ((), ())), preferred_element_type=jnp.float32
    )
    return (grad_gate, grad_up, grad_down)


def local(tokens, cotangent, expert_ids, gate_probs, w_gate, w_up, w_down):
    owners = lax.axis_size("expert")
    tok_rows = tokens.shape[0]
    model_width = tokens.shape[1]
    fanout = expert_ids.shape[1]
    capacity = max(2, 2 * tok_rows * fanout // owners)
    copies = tok_rows * fanout
    flat_ids = expert_ids.reshape(copies)
    onehot = (flat_ids[:, None] == jnp.arange(owners, dtype=jnp.int32)[None, :]).astype(jnp.int32)
    before = jnp.cumsum(onehot, axis=0) - onehot
    slot_rank = jnp.sum(before * onehot, axis=1)
    position = flat_ids * capacity + slot_rank
    copy_rows = tokens[:, None, :].reshape(copies, model_width)
    copy_tok_cot = cotangent[:, None, :].reshape(copies, model_width)
    copy_cots = (gate_probs * copy_tok_cot.astype(jnp.float32)).astype(jnp.bfloat16)
    placing = (jnp.arange(owners * capacity, dtype=jnp.int32)[:, None] == position[None, :]).astype(
        jnp.bfloat16
    )
    joined = jnp.concatenate([copy_rows, copy_cots], axis=1)
    sent = (
        jnp.dot(placing, joined, preferred_element_type=jnp.float32)
        .astype(jnp.bfloat16)
        .reshape(owners, capacity, 2 * model_width)
    )
    came = lax.all_to_all(sent, "expert", split_axis=0, concat_axis=0, tiled=True)
    swap = [(0, 1), (1, 0)]
    other = lax.ppermute(came, "dp", swap)
    half_slots = owners * capacity
    weights_own = (w_gate[0], w_up[0], w_down[0])
    came = came.reshape(half_slots, 2 * model_width)
    own_x = came[:, :model_width]
    own_cot = came[:, model_width:]
    own_h, own_dg, own_du = front_rows(own_x, own_cot, *weights_own)[:3]
    other = other.reshape(half_slots, 2 * model_width)
    oth_x = other[:, :model_width]
    oth_cot = other[:, model_width:]
    oth_h, oth_dg, oth_du, oth_dx = front_rows(oth_x, oth_cot, *weights_own)
    back = lax.ppermute(oth_dx, "dp", swap)
    own_dx = lax.optimization_barrier(input_grads(own_dg, own_du, weights_own[0], weights_own[1]))
    summed = (own_dx.astype(jnp.float32) + back.astype(jnp.float32)).astype(jnp.bfloat16)
    returned = lax.all_to_all(
        summed.reshape(owners, capacity, model_width), "expert", split_axis=0, concat_axis=0, tiled=True
    )
    sums_own = weight_sums(own_x, own_cot, own_h, own_dg, own_du)
    sums_oth = weight_sums(oth_x, oth_cot, oth_h, oth_dg, oth_du)
    grad_gate, grad_up, grad_down = (a + b for a, b in zip(sums_own, sums_oth))
    copy_grad = jnp.take(
        returned.reshape(owners * capacity, model_width), position, axis=0, mode="clip"
    )
    grad_tokens = jnp.sum(
        copy_grad.reshape(tok_rows, fanout, model_width).astype(jnp.float32), axis=1
    ).astype(jnp.bfloat16)
    return (
        grad_tokens,
        grad_gate.astype(jnp.bfloat16)[None],
        grad_up.astype(jnp.bfloat16)[None],
        grad_down.astype(jnp.bfloat16)[None],
    )


def solution(mesh):
    return jax.shard_map(
        local,
        mesh=mesh,
        in_specs=(
            P(("dp", "expert"), None),
            P(("dp", "expert"), None),
            P(("dp", "expert"), None),
            P(("dp", "expert"), None),
            P("expert", None, "dp"),
            P("expert", None, "dp"),
            P("expert", "dp", None),
        ),
        out_specs=(
            P(("dp", "expert"), None),
            P("expert", None, "dp"),
            P("expert", None, "dp"),
            P("expert", "dp", None),
        ),
        check_vma=False,
    )
```

```python
import jax
import jax.numpy as jnp
from jax import lax
from jax.sharding import PartitionSpec as P


def front_rows(rows_x, rows_cot, gate_w, up_w, down_w):
    gate_pre = jnp.dot(rows_x, gate_w, preferred_element_type=jnp.float32)
    up_pre = jnp.dot(rows_x, up_w, preferred_element_type=jnp.float32)
    sigmoid_gate = jax.nn.sigmoid(gate_pre)
    swish_gate = gate_pre * sigmoid_gate
    hidden = (swish_gate * up_pre).astype(jnp.bfloat16)
    d_hidden = lax.dot_general(
        rows_cot, down_w, (((1,), (1,)), ((), ())), preferred_element_type=jnp.float32
    )
    d_gate = (d_hidden * up_pre * sigmoid_gate * (1.0 + gate_pre * (1.0 - sigmoid_gate))).astype(
        jnp.bfloat16
    )
    d_up = (d_hidden * swish_gate).astype(jnp.bfloat16)
    return (hidden, d_gate, d_up, input_grads(d_gate, d_up, gate_w, up_w))


def input_grads(d_gate, d_up, gate_w, up_w):
    dx_part = lax.dot_general(
        d_gate, gate_w, (((1,), (1,)), ((), ())), preferred_element_type=jnp.float32
    )
    dx_part = dx_part + lax.dot_general(
        d_up, up_w, (((1,), (1,)), ((), ())), preferred_element_type=jnp.float32
    )
    return dx_part.astype(jnp.bfloat16)


def weight_sums(rows_x, rows_cot, hidden, d_gate, d_up):
    grad_gate = lax.dot_general(
        rows_x, d_gate, (((0,), (0,)), ((), ())), preferred_element_type=jnp.float32
    )
    grad_up = lax.dot_general(
        rows_x, d_up, (((0,), (0,)), ((), ())), preferred_element_type=jnp.float32
    )
    grad_down = lax.dot_general(
        hidden, rows_cot, (((0,), (0,)), ((), ())), preferred_element_type=jnp.float32
    )
    return (grad_gate, grad_up, grad_down)


def local(tokens, cotangent, expert_ids, gate_probs, w_gate, w_up, w_down):
    owners = lax.axis_size("expert")
    tok_rows = tokens.shape[0]
    model_width = tokens.shape[1]
    fanout = expert_ids.shape[1]
    capacity = max(2, 2 * tok_rows * fanout // owners)
    copies = tok_rows * fanout
    flat_ids = expert_ids.reshape(copies)
    onehot = (flat_ids[:, None] == jnp.arange(owners, dtype=jnp.int32)[None, :]).astype(jnp.int32)
    before = jnp.cumsum(onehot, axis=0) - onehot
    slot_rank = jnp.sum(before * onehot, axis=1)
    position = flat_ids * capacity + slot_rank
    copy_rows = tokens[:, None, :].reshape(copies, model_width)
    copy_tok_cot = cotangent[:, None, :].reshape(copies, model_width)
    copy_cots = (gate_probs * copy_tok_cot.astype(jnp.float32)).astype(jnp.bfloat16)
    placing = (jnp.arange(owners * capacity, dtype=jnp.int32)[:, None] == position[None, :]).astype(
        jnp.bfloat16
    )
    joined = jnp.concatenate([copy_rows, copy_cots], axis=1)
    sent = (
        jnp.dot(placing, joined, preferred_element_type=jnp.float32)
        .astype(jnp.bfloat16)
        .reshape(owners, capacity, 2 * model_width)
    )
    came = lax.all_to_all(sent, "expert", split_axis=0, concat_axis=0, tiled=True)
    swap = [(0, 1), (1, 0)]
    other = lax.ppermute(came, "dp", swap)
    half_slots = owners * capacity
    weights_own = (w_gate[0], w_up[0], w_down[0])
    came = came.reshape(half_slots, 2 * model_width)
    own_x = came[:, :model_width]
    own_cot = came[:, model_width:]
    own_h, own_dg, own_du = front_rows(own_x, own_cot, *weights_own)[:3]
    other = other.reshape(half_slots, 2 * model_width)
    oth_x = other[:, :model_width]
    oth_cot = other[:, model_width:]
    oth_h, oth_dg, oth_du, oth_dx = front_rows(oth_x, oth_cot, *weights_own)
    back = lax.ppermute(oth_dx, "dp", swap)
    own_dx = lax.dot_general(
        own_dg, weights_own[0], (((1,), (1,)), ((), ())), preferred_element_type=jnp.float32
    )
    own_dx = own_dx + lax.dot_general(
        own_du, weights_own[1], (((1,), (1,)), ((), ())), preferred_element_type=jnp.float32
    )
    summed = (own_dx + back.astype(jnp.float32)).astype(jnp.bfloat16)
    returned = lax.all_to_all(
        summed.reshape(owners, capacity, model_width), "expert", split_axis=0, concat_axis=0, tiled=True
    )
    sums_own = weight_sums(own_x, own_cot, own_h, own_dg, own_du)
    sums_oth = weight_sums(oth_x, oth_cot, oth_h, oth_dg, oth_du)
    grad_gate, grad_up, grad_down = (a + b for a, b in zip(sums_own, sums_oth))
    copy_grad = lax.dot_general(
        placing,
        returned.reshape(owners * capacity, model_width),
        (((0,), (0,)), ((), ())),
        preferred_element_type=jnp.float32,
    )
    grad_tokens = jnp.sum(copy_grad.reshape(tok_rows, fanout, model_width), axis=1).astype(
        jnp.bfloat16
    )
    return (
        grad_tokens,
        grad_gate.astype(jnp.bfloat16)[None],
        grad_up.astype(jnp.bfloat16)[None],
        grad_down.astype(jnp.bfloat16)[None],
    )


def solution(mesh):
    return jax.shard_map(
        local,
        mesh=mesh,
        in_specs=(
            P(("dp", "expert"), None),
            P(("dp", "expert"), None),
            P(("dp", "expert"), None),
            P(("dp", "expert"), None),
            P("expert", None, "dp"),
            P("expert", None, "dp"),
            P("expert", "dp", None),
        ),
        out_specs=(
            P(("dp", "expert"), None),
            P("expert", None, "dp"),
            P("expert", None, "dp"),
            P("expert", "dp", None),
        ),
        check_vma=False,
    )
```

```python
import jax
import jax.numpy as jnp
from jax import lax
from jax.sharding import PartitionSpec as P


def front_rows(rows_x, rows_cot, gate_w, up_w, down_w):
    gate_pre = jnp.dot(rows_x, gate_w, preferred_element_type=jnp.float32)
    up_pre = jnp.dot(rows_x, up_w, preferred_element_type=jnp.float32)
    sigmoid_gate = jax.nn.sigmoid(gate_pre)
    swish_gate = gate_pre * sigmoid_gate
    hidden = (swish_gate * up_pre).astype(jnp.bfloat16)
    d_hidden = lax.dot_general(
        rows_cot, down_w, (((1,), (1,)), ((), ())), preferred_element_type=jnp.float32
    )
    d_gate = (d_hidden * up_pre * sigmoid_gate * (1.0 + gate_pre * (1.0 - sigmoid_gate))).astype(
        jnp.bfloat16
    )
    d_up = (d_hidden * swish_gate).astype(jnp.bfloat16)
    return (hidden, d_gate, d_up, input_grads(d_gate, d_up, gate_w, up_w))


def input_grads(d_gate, d_up, gate_w, up_w):
    dx_part = lax.dot_general(
        d_gate, gate_w, (((1,), (1,)), ((), ())), preferred_element_type=jnp.float32
    )
    dx_part = dx_part + lax.dot_general(
        d_up, up_w, (((1,), (1,)), ((), ())), preferred_element_type=jnp.float32
    )
    return dx_part.astype(jnp.bfloat16)


def weight_sums(rows_x, rows_cot, hidden, d_gate, d_up):
    grad_gate = lax.dot_general(
        rows_x, d_gate, (((0,), (0,)), ((), ())), preferred_element_type=jnp.float32
    )
    grad_up = lax.dot_general(
        rows_x, d_up, (((0,), (0,)), ((), ())), preferred_element_type=jnp.float32
    )
    grad_down = lax.dot_general(
        hidden, rows_cot, (((0,), (0,)), ((), ())), preferred_element_type=jnp.float32
    )
    return (grad_gate, grad_up, grad_down)


def local(tokens, cotangent, expert_ids, gate_probs, w_gate, w_up, w_down):
    owners = lax.axis_size("expert")
    tok_rows = tokens.shape[0]
    model_width = tokens.shape[1]
    fanout = expert_ids.shape[1]
    capacity = max(2, 2 * tok_rows * fanout // owners)
    copies = tok_rows * fanout
    flat_ids = expert_ids.reshape(copies)
    onehot = (flat_ids[:, None] == jnp.arange(owners, dtype=jnp.int32)[None, :]).astype(jnp.int32)
    before = jnp.cumsum(onehot, axis=0) - onehot
    slot_rank = jnp.sum(before * onehot, axis=1)
    position = flat_ids * capacity + slot_rank
    copy_rows = tokens[:, None, :].reshape(copies, model_width)
    copy_tok_cot = cotangent[:, None, :].reshape(copies, model_width)
    copy_cots = (gate_probs * copy_tok_cot.astype(jnp.float32)).astype(jnp.bfloat16)
    placing = (jnp.arange(owners * capacity, dtype=jnp.int32)[:, None] == position[None, :]).astype(
        jnp.bfloat16
    )
    joined = jnp.concatenate([copy_rows, copy_cots], axis=1)
    sent = (
        jnp.dot(placing, joined, preferred_element_type=jnp.float32)
        .astype(jnp.bfloat16)
        .reshape(owners, capacity, 2 * model_width)
    )
    came = lax.all_to_all(sent, "expert", split_axis=0, concat_axis=0, tiled=True)
    swap = [(0, 1), (1, 0)]
    other = lax.ppermute(came, "dp", swap)
    half_slots = owners * capacity
    weights_own = (w_gate[0], w_up[0], w_down[0])
    came = came.reshape(half_slots, 2 * model_width)
    own_x = came[:, :model_width]
    own_cot = came[:, model_width:]
    own_h, own_dg, own_du = front_rows(own_x, own_cot, *weights_own)[:3]
    other = other.reshape(half_slots, 2 * model_width)
    oth_x = other[:, :model_width]
    oth_cot = other[:, model_width:]
    oth_h, oth_dg, oth_du, oth_dx = front_rows(oth_x, oth_cot, *weights_own)
    back = lax.ppermute(oth_dx, "dp", swap)
    own_dx = lax.dot_general(
        own_dg, weights_own[0], (((1,), (1,)), ((), ())), preferred_element_type=jnp.float32
    )
    own_dx = own_dx + lax.dot_general(
        own_du, weights_own[1], (((1,), (1,)), ((), ())), preferred_element_type=jnp.float32
    )
    summed = (own_dx + back.astype(jnp.float32)).astype(jnp.bfloat16)
    returned = lax.all_to_all(
        summed.reshape(owners, capacity, model_width), "expert", split_axis=0, concat_axis=0, tiled=True
    )
    sums_own = weight_sums(own_x, own_cot, own_h, own_dg, own_du)
    sums_oth = weight_sums(oth_x, oth_cot, oth_h, oth_dg, oth_du)
    grad_gate, grad_up, grad_down = (a + b for a, b in zip(sums_own, sums_oth))
    gathering = (position[:, None] == jnp.arange(owners * capacity, dtype=jnp.int32)[None, :]).astype(
        jnp.bfloat16
    )
    copy_grad = jnp.dot(
        gathering,
        returned.reshape(owners * capacity, model_width),
        preferred_element_type=jnp.float32,
    )
    grad_tokens = jnp.sum(copy_grad.reshape(tok_rows, fanout, model_width), axis=1).astype(
        jnp.bfloat16
    )
    return (
        grad_tokens,
        grad_gate.astype(jnp.bfloat16)[None],
        grad_up.astype(jnp.bfloat16)[None],
        grad_down.astype(jnp.bfloat16)[None],
    )


def solution(mesh):
    return jax.shard_map(
        local,
        mesh=mesh,
        in_specs=(
            P(("dp", "expert"), None),
            P(("dp", "expert"), None),
            P(("dp", "expert"), None),
            P(("dp", "expert"), None),
            P("expert", None, "dp"),
            P("expert", None, "dp"),
            P("expert", "dp", None),
        ),
        out_specs=(
            P(("dp", "expert"), None),
            P("expert", None, "dp"),
            P("expert", None, "dp"),
            P("expert", "dp", None),
        ),
        check_vma=False,
    )
```

```python
import jax
import jax.numpy as jnp
from jax import lax
from jax.sharding import PartitionSpec as P


def front_rows(rows_x, rows_cot, gate_w, up_w, down_w):
    gate_pre = jnp.dot(rows_x, gate_w, preferred_element_type=jnp.float32)
    up_pre = jnp.dot(rows_x, up_w, preferred_element_type=jnp.float32)
    sigmoid_gate = jax.nn.sigmoid(gate_pre)
    swish_gate = gate_pre * sigmoid_gate
    hidden = (swish_gate * up_pre).astype(jnp.bfloat16)
    d_hidden = lax.dot_general(
        rows_cot, down_w, (((1,), (1,)), ((), ())), preferred_element_type=jnp.float32
    )
    d_gate = (d_hidden * up_pre * sigmoid_gate * (1.0 + gate_pre * (1.0 - sigmoid_gate))).astype(
        jnp.bfloat16
    )
    d_up = (d_hidden * swish_gate).astype(jnp.bfloat16)
    return (hidden, d_gate, d_up, input_grads(d_gate, d_up, gate_w, up_w))


def input_grads(d_gate, d_up, gate_w, up_w):
    dx_part = lax.dot_general(
        d_gate, gate_w, (((1,), (1,)), ((), ())), preferred_element_type=jnp.float32
    )
    dx_part = dx_part + lax.dot_general(
        d_up, up_w, (((1,), (1,)), ((), ())), preferred_element_type=jnp.float32
    )
    return dx_part.astype(jnp.bfloat16)


def weight_sums(rows_x, rows_cot, hidden, d_gate, d_up):
    grad_gate = lax.dot_general(
        rows_x, d_gate, (((0,), (0,)), ((), ())), preferred_element_type=jnp.float32
    )
    grad_up = lax.dot_general(
        rows_x, d_up, (((0,), (0,)), ((), ())), preferred_element_type=jnp.float32
    )
    grad_down = lax.dot_general(
        hidden, rows_cot, (((0,), (0,)), ((), ())), preferred_element_type=jnp.float32
    )
    return (grad_gate, grad_up, grad_down)


def local(tokens, cotangent, expert_ids, gate_probs, w_gate, w_up, w_down):
    owners = lax.axis_size("expert")
    tok_rows = tokens.shape[0]
    model_width = tokens.shape[1]
    fanout = expert_ids.shape[1]
    capacity = max(2, 2 * tok_rows * fanout // owners)
    copies = tok_rows * fanout
    flat_ids = expert_ids.reshape(copies)
    onehot = (flat_ids[:, None] == jnp.arange(owners, dtype=jnp.int32)[None, :]).astype(jnp.int32)
    before = jnp.cumsum(onehot, axis=0) - onehot
    slot_rank = jnp.sum(before * onehot, axis=1)
    position = flat_ids * capacity + slot_rank
    copy_rows = tokens[:, None, :].reshape(copies, model_width)
    copy_tok_cot = cotangent[:, None, :].reshape(copies, model_width)
    copy_cots = (gate_probs * copy_tok_cot.astype(jnp.float32)).astype(jnp.bfloat16)
    placing = (jnp.arange(owners * capacity, dtype=jnp.int32)[:, None] == position[None, :]).astype(
        jnp.bfloat16
    )
    joined = jnp.concatenate([copy_rows, copy_cots], axis=1)
    sent = (
        jnp.dot(placing, joined, preferred_element_type=jnp.float32)
        .astype(jnp.bfloat16)
        .reshape(owners, capacity, 2 * model_width)
    )
    came = lax.all_to_all(sent, "expert", split_axis=0, concat_axis=0, tiled=True)
    swap = [(0, 1), (1, 0)]
    other = lax.ppermute(came, "dp", swap)
    half_slots = owners * capacity
    weights_own = (w_gate[0], w_up[0], w_down[0])
    came = came.reshape(half_slots, 2 * model_width)
    own_x = came[:, :model_width]
    own_cot = came[:, model_width:]
    own_h, own_dg, own_du = front_rows(own_x, own_cot, *weights_own)[:3]
    other = other.reshape(half_slots, 2 * model_width)
    oth_x = other[:, :model_width]
    oth_cot = other[:, model_width:]
    oth_h, oth_dg, oth_du = front_rows(oth_x, oth_cot, *weights_own)[:3]
    split = half_slots // 2
    dx_first = input_grads(oth_dg[:split], oth_du[:split], weights_own[0], weights_own[1])
    back_first = lax.ppermute(dx_first, "dp", swap)
    dx_second = input_grads(oth_dg[split:], oth_du[split:], weights_own[0], weights_own[1])
    back_second = lax.ppermute(dx_second, "dp", swap)
    back = jnp.concatenate([back_first, back_second], axis=0)
    own_dx = lax.dot_general(
        own_dg, weights_own[0], (((1,), (1,)), ((), ())), preferred_element_type=jnp.float32
    )
    own_dx = own_dx + lax.dot_general(
        own_du, weights_own[1], (((1,), (1,)), ((), ())), preferred_element_type=jnp.float32
    )
    summed = (own_dx + back.astype(jnp.float32)).astype(jnp.bfloat16)
    returned = lax.all_to_all(
        summed.reshape(owners, capacity, model_width), "expert", split_axis=0, concat_axis=0, tiled=True
    )
    sums_own = weight_sums(own_x, own_cot, own_h, own_dg, own_du)
    sums_oth = weight_sums(oth_x, oth_cot, oth_h, oth_dg, oth_du)
    grad_gate, grad_up, grad_down = (a + b for a, b in zip(sums_own, sums_oth))
    gathering = lax.optimization_barrier(
        (position[:, None] == jnp.arange(owners * capacity, dtype=jnp.int32)[None, :]).astype(
            jnp.bfloat16
        )
    )
    copy_grad = jnp.dot(
        gathering,
        returned.reshape(owners * capacity, model_width),
        preferred_element_type=jnp.float32,
    )
    grad_tokens = jnp.sum(copy_grad.reshape(tok_rows, fanout, model_width), axis=1).astype(
        jnp.bfloat16
    )
    return (
        grad_tokens,
        grad_gate.astype(jnp.bfloat16)[None],
        grad_up.astype(jnp.bfloat16)[None],
        grad_down.astype(jnp.bfloat16)[None],
    )


def solution(mesh):
    return jax.shard_map(
        local,
        mesh=mesh,
        in_specs=(
            P(("dp", "expert"), None),
            P(("dp", "expert"), None),
            P(("dp", "expert"), None),
            P(("dp", "expert"), None),
            P("expert", None, "dp"),
            P("expert", None, "dp"),
            P("expert", "dp", None),
        ),
        out_specs=(
            P(("dp", "expert"), None),
            P("expert", None, "dp"),
            P("expert", None, "dp"),
            P("expert", "dp", None),
        ),
        check_vma=False,
    )
```

```python
import jax
import jax.numpy as jnp
from jax import lax
from jax.sharding import PartitionSpec as P


def front_rows(rows_x, rows_cot, gate_w, up_w, down_w):
    gate_pre = jnp.dot(rows_x, gate_w, preferred_element_type=jnp.float32)
    up_pre = jnp.dot(rows_x, up_w, preferred_element_type=jnp.float32)
    sigmoid_gate = jax.nn.sigmoid(gate_pre)
    swish_gate = gate_pre * sigmoid_gate
    hidden = (swish_gate * up_pre).astype(jnp.bfloat16)
    d_hidden = lax.dot_general(
        rows_cot, down_w, (((1,), (1,)), ((), ())), preferred_element_type=jnp.float32
    )
    d_gate = (d_hidden * up_pre * sigmoid_gate * (1.0 + gate_pre * (1.0 - sigmoid_gate))).astype(
        jnp.bfloat16
    )
    d_up = (d_hidden * swish_gate).astype(jnp.bfloat16)
    return (hidden, d_gate, d_up, input_grads(d_gate, d_up, gate_w, up_w))


def input_grads(d_gate, d_up, gate_w, up_w):
    dx_part = lax.dot_general(
        d_gate, gate_w, (((1,), (1,)), ((), ())), preferred_element_type=jnp.float32
    )
    dx_part = dx_part + lax.dot_general(
        d_up, up_w, (((1,), (1,)), ((), ())), preferred_element_type=jnp.float32
    )
    return dx_part.astype(jnp.bfloat16)


def weight_sums(rows_x, rows_cot, hidden, d_gate, d_up):
    grad_gate = lax.dot_general(
        rows_x, d_gate, (((0,), (0,)), ((), ())), preferred_element_type=jnp.float32
    )
    grad_up = lax.dot_general(
        rows_x, d_up, (((0,), (0,)), ((), ())), preferred_element_type=jnp.float32
    )
    grad_down = lax.dot_general(
        hidden, rows_cot, (((0,), (0,)), ((), ())), preferred_element_type=jnp.float32
    )
    return (grad_gate, grad_up, grad_down)


def local(tokens, cotangent, expert_ids, gate_probs, w_gate, w_up, w_down):
    owners = lax.axis_size("expert")
    tok_rows = tokens.shape[0]
    model_width = tokens.shape[1]
    fanout = expert_ids.shape[1]
    capacity = max(2, 2 * tok_rows * fanout // owners)
    copies = tok_rows * fanout
    flat_ids = expert_ids.reshape(copies)
    onehot = (flat_ids[:, None] == jnp.arange(owners, dtype=jnp.int32)[None, :]).astype(jnp.bfloat16)
    order = jnp.arange(copies, dtype=jnp.int32)
    earlier = (order[None, :] < order[:, None]).astype(jnp.bfloat16)
    before = jnp.dot(earlier, onehot, preferred_element_type=jnp.float32)
    slot_rank = jnp.sum(before * onehot.astype(jnp.float32), axis=1).astype(jnp.int32)
    position = flat_ids * capacity + slot_rank
    copy_rows = tokens[:, None, :].reshape(copies, model_width)
    copy_tok_cot = cotangent[:, None, :].reshape(copies, model_width)
    copy_cots = (gate_probs * copy_tok_cot.astype(jnp.float32)).astype(jnp.bfloat16)
    placing = (jnp.arange(owners * capacity, dtype=jnp.int32)[:, None] == position[None, :]).astype(
        jnp.bfloat16
    )
    joined = jnp.concatenate([copy_rows, copy_cots], axis=1)
    sent = (
        jnp.dot(placing, joined, preferred_element_type=jnp.float32)
        .astype(jnp.bfloat16)
        .reshape(owners, capacity, 2 * model_width)
    )
    came = lax.all_to_all(sent, "expert", split_axis=0, concat_axis=0, tiled=True)
    swap = [(0, 1), (1, 0)]
    other = lax.ppermute(came, "dp", swap)
    half_slots = owners * capacity
    weights_own = (w_gate[0], w_up[0], w_down[0])
    came = came.reshape(half_slots, 2 * model_width)
    own_x = came[:, :model_width]
    own_cot = came[:, model_width:]
    own_h, own_dg, own_du = front_rows(own_x, own_cot, *weights_own)[:3]
    other = other.reshape(half_slots, 2 * model_width)
    oth_x = other[:, :model_width]
    oth_cot = other[:, model_width:]
    oth_h, oth_dg, oth_du = front_rows(oth_x, oth_cot, *weights_own)[:3]
    split = half_slots // 2
    dx_first = input_grads(oth_dg[:split], oth_du[:split], weights_own[0], weights_own[1])
    back_first = lax.ppermute(dx_first, "dp", swap)
    dx_second = input_grads(oth_dg[split:], oth_du[split:], weights_own[0], weights_own[1])
    back_second = lax.ppermute(dx_second, "dp", swap)
    back = jnp.concatenate([back_first, back_second], axis=0)
    own_dx = lax.dot_general(
        own_dg, weights_own[0], (((1,), (1,)), ((), ())), preferred_element_type=jnp.float32
    )
    own_dx = own_dx + lax.dot_general(
        own_du, weights_own[1], (((1,), (1,)), ((), ())), preferred_element_type=jnp.float32
    )
    summed = (own_dx + back.astype(jnp.float32)).astype(jnp.bfloat16)
    returned = lax.all_to_all(
        summed.reshape(owners, capacity, model_width), "expert", split_axis=0, concat_axis=0, tiled=True
    )
    sums_own = weight_sums(own_x, own_cot, own_h, own_dg, own_du)
    sums_oth = weight_sums(oth_x, oth_cot, oth_h, oth_dg, oth_du)
    grad_gate, grad_up, grad_down = (a + b for a, b in zip(sums_own, sums_oth))
    gathering = lax.optimization_barrier(
        (position[:, None] == jnp.arange(owners * capacity, dtype=jnp.int32)[None, :]).astype(
            jnp.bfloat16
        )
    )
    copy_grad = jnp.dot(
        gathering,
        returned.reshape(owners * capacity, model_width),
        preferred_element_type=jnp.float32,
    )
    grad_tokens = jnp.sum(copy_grad.reshape(tok_rows, fanout, model_width), axis=1).astype(
        jnp.bfloat16
    )
    return (
        grad_tokens,
        grad_gate.astype(jnp.bfloat16)[None],
        grad_up.astype(jnp.bfloat16)[None],
        grad_down.astype(jnp.bfloat16)[None],
    )


def solution(mesh):
    return jax.shard_map(
        local,
        mesh=mesh,
        in_specs=(
            P(("dp", "expert"), None),
            P(("dp", "expert"), None),
            P(("dp", "expert"), None),
            P(("dp", "expert"), None),
            P("expert", None, "dp"),
            P("expert", None, "dp"),
            P("expert", "dp", None),
        ),
        out_specs=(
            P(("dp", "expert"), None),
            P("expert", None, "dp"),
            P("expert", None, "dp"),
            P("expert", "dp", None),
        ),
        check_vma=False,
    )
```

```python
import jax
import jax.numpy as jnp
from jax import lax
from jax.sharding import PartitionSpec as P


def front_rows(rows_x, rows_cot, gate_w, up_w, down_w):
    gate_pre = jnp.dot(rows_x, gate_w, preferred_element_type=jnp.float32)
    up_pre = jnp.dot(rows_x, up_w, preferred_element_type=jnp.float32)
    sigmoid_gate = jax.nn.sigmoid(gate_pre)
    swish_gate = gate_pre * sigmoid_gate
    hidden = (swish_gate * up_pre).astype(jnp.bfloat16)
    d_hidden = lax.dot_general(
        rows_cot, down_w, (((1,), (1,)), ((), ())), preferred_element_type=jnp.float32
    )
    d_gate = (d_hidden * up_pre * sigmoid_gate * (1.0 + gate_pre * (1.0 - sigmoid_gate))).astype(
        jnp.bfloat16
    )
    d_up = (d_hidden * swish_gate).astype(jnp.bfloat16)
    return (hidden, d_gate, d_up, input_grads(d_gate, d_up, gate_w, up_w))


def input_grads(d_gate, d_up, gate_w, up_w):
    dx_part = lax.dot_general(
        d_gate, gate_w, (((1,), (1,)), ((), ())), preferred_element_type=jnp.float32
    )
    dx_part = dx_part + lax.dot_general(
        d_up, up_w, (((1,), (1,)), ((), ())), preferred_element_type=jnp.float32
    )
    return dx_part.astype(jnp.bfloat16)


def weight_sums(rows_x, rows_cot, hidden, d_gate, d_up):
    grad_gate = lax.dot_general(
        rows_x, d_gate, (((0,), (0,)), ((), ())), preferred_element_type=jnp.float32
    )
    grad_up = lax.dot_general(
        rows_x, d_up, (((0,), (0,)), ((), ())), preferred_element_type=jnp.float32
    )
    grad_down = lax.dot_general(
        hidden, rows_cot, (((0,), (0,)), ((), ())), preferred_element_type=jnp.float32
    )
    return (grad_gate, grad_up, grad_down)


def local(tokens, cotangent, expert_ids, gate_probs, w_gate, w_up, w_down):
    owners = lax.axis_size("expert")
    tok_rows = tokens.shape[0]
    model_width = tokens.shape[1]
    fanout = expert_ids.shape[1]
    capacity = max(2, 2 * tok_rows * fanout // owners)
    copies = tok_rows * fanout
    flat_ids = expert_ids.reshape(copies)
    onehot = (flat_ids[:, None] == jnp.arange(owners, dtype=jnp.int32)[None, :]).astype(jnp.bfloat16)
    order = jnp.arange(copies, dtype=jnp.int32)
    earlier = (order[None, :] < order[:, None]).astype(jnp.bfloat16)
    before = jnp.dot(earlier, onehot, preferred_element_type=jnp.float32)
    slot_rank = jnp.sum(before * onehot.astype(jnp.float32), axis=1).astype(jnp.int32)
    position = flat_ids * capacity + slot_rank
    copy_rows = tokens[:, None, :].reshape(copies, model_width)
    copy_tok_cot = cotangent[:, None, :].reshape(copies, model_width)
    placing = (jnp.arange(owners * capacity, dtype=jnp.int32)[:, None] == position[None, :]).astype(
        jnp.bfloat16
    )
    joined = jnp.concatenate([copy_rows, copy_tok_cot], axis=1)
    slot_gate = jnp.sum(placing.astype(jnp.float32) * gate_probs.reshape(1, copies), axis=1)
    picked = jnp.dot(placing, joined, preferred_element_type=jnp.float32)
    is_cot = jnp.arange(2 * model_width, dtype=jnp.int32)[None, :] >= model_width
    sent = (
        jnp.where(is_cot, picked * slot_gate[:, None], picked)
        .astype(jnp.bfloat16)
        .reshape(owners, capacity, 2 * model_width)
    )
    came = lax.all_to_all(sent, "expert", split_axis=0, concat_axis=0, tiled=True)
    swap = [(0, 1), (1, 0)]
    other = lax.ppermute(came, "dp", swap)
    half_slots = owners * capacity
    weights_own = (w_gate[0], w_up[0], w_down[0])
    came = came.reshape(half_slots, 2 * model_width)
    own_x = came[:, :model_width]
    own_cot = came[:, model_width:]
    own_h, own_dg, own_du = front_rows(own_x, own_cot, *weights_own)[:3]
    other = other.reshape(half_slots, 2 * model_width)
    oth_x = other[:, :model_width]
    oth_cot = other[:, model_width:]
    oth_h, oth_dg, oth_du = front_rows(oth_x, oth_cot, *weights_own)[:3]
    split = half_slots // 2
    dx_first = input_grads(oth_dg[:split], oth_du[:split], weights_own[0], weights_own[1])
    back_first = lax.ppermute(dx_first, "dp", swap)
    dx_second = input_grads(oth_dg[split:], oth_du[split:], weights_own[0], weights_own[1])
    back_second = lax.ppermute(dx_second, "dp", swap)
    back = jnp.concatenate([back_first, back_second], axis=0)
    own_dx = lax.dot_general(
        own_dg, weights_own[0], (((1,), (1,)), ((), ())), preferred_element_type=jnp.float32
    )
    own_dx = own_dx + lax.dot_general(
        own_du, weights_own[1], (((1,), (1,)), ((), ())), preferred_element_type=jnp.float32
    )
    summed = (own_dx + back.astype(jnp.float32)).astype(jnp.bfloat16)
    returned = lax.all_to_all(
        summed.reshape(owners, capacity, model_width), "expert", split_axis=0, concat_axis=0, tiled=True
    )
    sums_own = weight_sums(own_x, own_cot, own_h, own_dg, own_du)
    sums_oth = weight_sums(oth_x, oth_cot, oth_h, oth_dg, oth_du)
    grad_gate, grad_up, grad_down = (a + b for a, b in zip(sums_own, sums_oth))
    gathering = lax.optimization_barrier(
        (position[:, None] == jnp.arange(owners * capacity, dtype=jnp.int32)[None, :]).astype(
            jnp.bfloat16
        )
    )
    copy_grad = jnp.dot(
        gathering,
        returned.reshape(owners * capacity, model_width),
        preferred_element_type=jnp.float32,
    )
    grad_tokens = jnp.sum(copy_grad.reshape(tok_rows, fanout, model_width), axis=1).astype(
        jnp.bfloat16
    )
    return (
        grad_tokens,
        grad_gate.astype(jnp.bfloat16)[None],
        grad_up.astype(jnp.bfloat16)[None],
        grad_down.astype(jnp.bfloat16)[None],
    )


def solution(mesh):
    return jax.shard_map(
        local,
        mesh=mesh,
        in_specs=(
            P(("dp", "expert"), None),
            P(("dp", "expert"), None),
            P(("dp", "expert"), None),
            P(("dp", "expert"), None),
            P("expert", None, "dp"),
            P("expert", None, "dp"),
            P("expert", "dp", None),
        ),
        out_specs=(
            P(("dp", "expert"), None),
            P("expert", None, "dp"),
            P("expert", None, "dp"),
            P("expert", "dp", None),
        ),
        check_vma=False,
    )
```

```python
import jax
import jax.numpy as jnp
from jax import lax
from jax.sharding import PartitionSpec as P


def front_rows(rows_x, rows_cot, gate_up_w, down_w):
    hidden_width = down_w.shape[0]
    both_pre = jnp.dot(rows_x, gate_up_w, preferred_element_type=jnp.float32)
    gate_pre = both_pre[:, :hidden_width]
    up_pre = both_pre[:, hidden_width:]
    sigmoid_gate = jax.nn.sigmoid(gate_pre)
    swish_gate = gate_pre * sigmoid_gate
    hidden = (swish_gate * up_pre).astype(jnp.bfloat16)
    d_hidden = lax.dot_general(
        rows_cot, down_w, (((1,), (1,)), ((), ())), preferred_element_type=jnp.float32
    )
    d_gate = (d_hidden * up_pre * sigmoid_gate * (1.0 + gate_pre * (1.0 - sigmoid_gate))).astype(
        jnp.bfloat16
    )
    d_up = (d_hidden * swish_gate).astype(jnp.bfloat16)
    return (hidden, d_gate, d_up)


def input_grads(d_gate, d_up, gate_up_w):
    both = jnp.concatenate([d_gate, d_up], axis=1)
    dx_part = lax.dot_general(
        both, gate_up_w, (((1,), (1,)), ((), ())), preferred_element_type=jnp.float32
    )
    return dx_part.astype(jnp.bfloat16)


def weight_sums(rows_x, rows_cot, hidden, d_gate, d_up):
    grad_gate = lax.dot_general(
        rows_x, d_gate, (((0,), (0,)), ((), ())), preferred_element_type=jnp.float32
    )
    grad_up = lax.dot_general(
        rows_x, d_up, (((0,), (0,)), ((), ())), preferred_element_type=jnp.float32
    )
    grad_down = lax.dot_general(
        hidden, rows_cot, (((0,), (0,)), ((), ())), preferred_element_type=jnp.float32
    )
    return (grad_gate, grad_up, grad_down)


def local(tokens, cotangent, expert_ids, gate_probs, w_gate, w_up, w_down):
    owners = lax.axis_size("expert")
    tok_rows = tokens.shape[0]
    model_width = tokens.shape[1]
    fanout = expert_ids.shape[1]
    capacity = max(2, 2 * tok_rows * fanout // owners)
    copies = tok_rows * fanout
    flat_ids = expert_ids.reshape(copies)
    onehot = (flat_ids[:, None] == jnp.arange(owners, dtype=jnp.int32)[None, :]).astype(jnp.bfloat16)
    order = jnp.arange(copies, dtype=jnp.int32)
    earlier = (order[None, :] < order[:, None]).astype(jnp.bfloat16)
    before = jnp.dot(earlier, onehot, preferred_element_type=jnp.float32)
    slot_rank = jnp.sum(before * onehot.astype(jnp.float32), axis=1).astype(jnp.int32)
    position = flat_ids * capacity + slot_rank
    copy_rows = tokens[:, None, :].reshape(copies, model_width)
    copy_tok_cot = cotangent[:, None, :].reshape(copies, model_width)
    copy_cots = (gate_probs * copy_tok_cot.astype(jnp.float32)).astype(jnp.bfloat16)
    placing = (jnp.arange(owners * capacity, dtype=jnp.int32)[:, None] == position[None, :]).astype(
        jnp.bfloat16
    )
    joined = jnp.concatenate([copy_rows, copy_cots], axis=1)
    sent = (
        jnp.dot(placing, joined, preferred_element_type=jnp.float32)
        .astype(jnp.bfloat16)
        .reshape(owners, capacity, 2 * model_width)
    )
    came = lax.all_to_all(sent, "expert", split_axis=0, concat_axis=0, tiled=True)
    swap = [(0, 1), (1, 0)]
    other = lax.ppermute(came, "dp", swap)
    half_slots = owners * capacity
    gate_up = jnp.concatenate([w_gate[0], w_up[0]], axis=1)
    weights_own = (gate_up, w_down[0])
    came = came.reshape(half_slots, 2 * model_width)
    own_x = came[:, :model_width]
    own_cot = came[:, model_width:]
    own_h, own_dg, own_du = front_rows(own_x, own_cot, *weights_own)
    other = other.reshape(half_slots, 2 * model_width)
    oth_x = other[:, :model_width]
    oth_cot = other[:, model_width:]
    oth_h, oth_dg, oth_du = front_rows(oth_x, oth_cot, *weights_own)
    split = half_slots // 2
    dx_first = input_grads(oth_dg[:split], oth_du[:split], gate_up)
    back_first = lax.ppermute(dx_first, "dp", swap)
    dx_second = input_grads(oth_dg[split:], oth_du[split:], gate_up)
    back_second = lax.ppermute(dx_second, "dp", swap)
    back = jnp.concatenate([back_first, back_second], axis=0)
    own_dx = lax.dot_general(
        jnp.concatenate([own_dg, own_du], axis=1),
        gate_up,
        (((1,), (1,)), ((), ())),
        preferred_element_type=jnp.float32,
    )
    summed = (own_dx + back.astype(jnp.float32)).astype(jnp.bfloat16)
    returned = lax.all_to_all(
        summed.reshape(owners, capacity, model_width), "expert", split_axis=0, concat_axis=0, tiled=True
    )
    sums_own = weight_sums(own_x, own_cot, own_h, own_dg, own_du)
    sums_oth = weight_sums(oth_x, oth_cot, oth_h, oth_dg, oth_du)
    grad_gate, grad_up, grad_down = (a + b for a, b in zip(sums_own, sums_oth))
    gathering = lax.optimization_barrier(
        (position[:, None] == jnp.arange(owners * capacity, dtype=jnp.int32)[None, :]).astype(
            jnp.bfloat16
        )
    )
    copy_grad = jnp.dot(
        gathering,
        returned.reshape(owners * capacity, model_width),
        preferred_element_type=jnp.float32,
    )
    grad_tokens = jnp.sum(copy_grad.reshape(tok_rows, fanout, model_width), axis=1).astype(
        jnp.bfloat16
    )
    return (
        grad_tokens,
        grad_gate.astype(jnp.bfloat16)[None],
        grad_up.astype(jnp.bfloat16)[None],
        grad_down.astype(jnp.bfloat16)[None],
    )


def solution(mesh):
    return jax.shard_map(
        local,
        mesh=mesh,
        in_specs=(
            P(("dp", "expert"), None),
            P(("dp", "expert"), None),
            P(("dp", "expert"), None),
            P(("dp", "expert"), None),
            P("expert", None, "dp"),
            P("expert", None, "dp"),
            P("expert", "dp", None),
        ),
        out_specs=(
            P(("dp", "expert"), None),
            P("expert", None, "dp"),
            P("expert", None, "dp"),
            P("expert", "dp", None),
        ),
        check_vma=False,
    )
```

```python
import jax
import jax.numpy as jnp
from jax import lax
from jax.sharding import PartitionSpec as P


def front_rows(rows_x, rows_cot, gate_w, up_w, down_w):
    gate_pre = jnp.dot(rows_x, gate_w, preferred_element_type=jnp.float32)
    up_pre = jnp.dot(rows_x, up_w, preferred_element_type=jnp.float32)
    sigmoid_gate = jax.nn.sigmoid(gate_pre)
    swish_gate = gate_pre * sigmoid_gate
    hidden = (swish_gate * up_pre).astype(jnp.bfloat16)
    d_hidden = lax.dot_general(
        rows_cot, down_w, (((1,), (1,)), ((), ())), preferred_element_type=jnp.float32
    )
    d_gate = (d_hidden * up_pre * sigmoid_gate * (1.0 + gate_pre * (1.0 - sigmoid_gate))).astype(
        jnp.bfloat16
    )
    d_up = (d_hidden * swish_gate).astype(jnp.bfloat16)
    return (hidden, d_gate, d_up, input_grads(d_gate, d_up, gate_w, up_w))


def input_grads(d_gate, d_up, gate_w, up_w):
    dx_part = lax.dot_general(
        d_gate, gate_w, (((1,), (1,)), ((), ())), preferred_element_type=jnp.float32
    )
    dx_part = dx_part + lax.dot_general(
        d_up, up_w, (((1,), (1,)), ((), ())), preferred_element_type=jnp.float32
    )
    return dx_part.astype(jnp.bfloat16)


def weight_sums(rows_x, rows_cot, hidden, d_gate, d_up):
    grad_gate = lax.dot_general(
        rows_x, d_gate, (((0,), (0,)), ((), ())), preferred_element_type=jnp.float32
    )
    grad_up = lax.dot_general(
        rows_x, d_up, (((0,), (0,)), ((), ())), preferred_element_type=jnp.float32
    )
    grad_down = lax.dot_general(
        hidden, rows_cot, (((0,), (0,)), ((), ())), preferred_element_type=jnp.float32
    )
    return (grad_gate, grad_up, grad_down)


def local(tokens, cotangent, expert_ids, gate_probs, w_gate, w_up, w_down):
    owners = lax.axis_size("expert")
    tok_rows = tokens.shape[0]
    model_width = tokens.shape[1]
    fanout = expert_ids.shape[1]
    capacity = max(2, 2 * tok_rows * fanout // owners)
    copies = tok_rows * fanout
    flat_ids = expert_ids.reshape(copies)
    onehot = (flat_ids[:, None] == jnp.arange(owners, dtype=jnp.int32)[None, :]).astype(jnp.bfloat16)
    order = jnp.arange(copies, dtype=jnp.int32)
    earlier = (order[None, :] < order[:, None]).astype(jnp.bfloat16)
    before = jnp.dot(earlier, onehot, preferred_element_type=jnp.float32)
    slot_rank = jnp.sum(before * onehot.astype(jnp.float32), axis=1).astype(jnp.int32)
    position = flat_ids * capacity + slot_rank
    copy_rows = tokens[:, None, :].reshape(copies, model_width)
    copy_tok_cot = cotangent[:, None, :].reshape(copies, model_width)
    copy_cots = (gate_probs * copy_tok_cot.astype(jnp.float32)).astype(jnp.bfloat16)
    placing = (jnp.arange(owners * capacity, dtype=jnp.int32)[:, None] == position[None, :]).astype(
        jnp.bfloat16
    )
    joined = jnp.concatenate([copy_rows, copy_cots], axis=1)
    sent = (
        jnp.dot(placing, joined, preferred_element_type=jnp.float32)
        .astype(jnp.bfloat16)
        .reshape(owners, capacity, 2 * model_width)
    )
    came = lax.all_to_all(sent, "expert", split_axis=0, concat_axis=0, tiled=True)
    swap = [(0, 1), (1, 0)]
    other = lax.ppermute(came, "dp", swap)
    half_slots = owners * capacity
    weights_own = (w_gate[0], w_up[0], w_down[0])
    came = came.reshape(half_slots, 2 * model_width)
    own_x = came[:, :model_width]
    own_cot = came[:, model_width:]
    own_h, own_dg, own_du = front_rows(own_x, own_cot, *weights_own)[:3]
    other = other.reshape(half_slots, 2 * model_width)
    oth_x = other[:, :model_width]
    oth_cot = other[:, model_width:]
    oth_h, oth_dg, oth_du = front_rows(oth_x, oth_cot, *weights_own)[:3]
    pieces = 4
    step = half_slots // pieces
    backs = []
    for piece in range(pieces):
        rows = slice(piece * step, (piece + 1) * step)
        dx_piece = input_grads(oth_dg[rows], oth_du[rows], weights_own[0], weights_own[1])
        backs.append(lax.ppermute(dx_piece, "dp", swap))
    back = jnp.concatenate(backs, axis=0)
    own_dx = lax.dot_general(
        own_dg, weights_own[0], (((1,), (1,)), ((), ())), preferred_element_type=jnp.float32
    )
    own_dx = own_dx + lax.dot_general(
        own_du, weights_own[1], (((1,), (1,)), ((), ())), preferred_element_type=jnp.float32
    )
    summed = (own_dx + back.astype(jnp.float32)).astype(jnp.bfloat16)
    returned = lax.all_to_all(
        summed.reshape(owners, capacity, model_width), "expert", split_axis=0, concat_axis=0, tiled=True
    )
    sums_own = weight_sums(own_x, own_cot, own_h, own_dg, own_du)
    sums_oth = weight_sums(oth_x, oth_cot, oth_h, oth_dg, oth_du)
    grad_gate, grad_up, grad_down = (a + b for a, b in zip(sums_own, sums_oth))
    gathering = lax.optimization_barrier(
        (position[:, None] == jnp.arange(owners * capacity, dtype=jnp.int32)[None, :]).astype(
            jnp.bfloat16
        )
    )
    copy_grad = jnp.dot(
        gathering,
        returned.reshape(owners * capacity, model_width),
        preferred_element_type=jnp.float32,
    )
    grad_tokens = jnp.sum(copy_grad.reshape(tok_rows, fanout, model_width), axis=1).astype(
        jnp.bfloat16
    )
    return (
        grad_tokens,
        grad_gate.astype(jnp.bfloat16)[None],
        grad_up.astype(jnp.bfloat16)[None],
        grad_down.astype(jnp.bfloat16)[None],
    )


def solution(mesh):
    return jax.shard_map(
        local,
        mesh=mesh,
        in_specs=(
            P(("dp", "expert"), None),
            P(("dp", "expert"), None),
            P(("dp", "expert"), None),
            P(("dp", "expert"), None),
            P("expert", None, "dp"),
            P("expert", None, "dp"),
            P("expert", "dp", None),
        ),
        out_specs=(
            P(("dp", "expert"), None),
            P("expert", None, "dp"),
            P("expert", None, "dp"),
            P("expert", "dp", None),
        ),
        check_vma=False,
    )
```
